512 devices in a mesh: vox: 32 (over y, x, core), tm: 16 (over z).
Axes of the slice: x: 4, y: 4, z: 16, core: 2. Of those that a mesh axis runs over, the one named last changes fastest.
Arguments:
- series: float32 [2048, 65536], P('tm', 'vox'), may hold values from -40 to 40
- spikes: int32 [2048, 65536], P('tm', 'vox'), may hold values from 0 to 15
- motion: float32 [2048, 6], P('tm'), may hold values from -5 to 5
- tissue: float32 [3, 65536], P(None, 'vox'), may hold values from 0.01 to 12, as said below
Outputs:
- cleaned: float32 [2048, 65536], P('tm', 'vox')
The draws below stay inside these ranges and needn't reach their ends.
Inputs may be any that keep to these rules, and one draw needn't show every extreme that they name: Bit j-1 of an entry (spikes // 2^(j-1) odd) flags that frame's level-j coefficient of that voxel as a spike. `tissue`: all weights are positive.
All inputs are finite; a program needn't handle non-finite values.
Results may differ from the reference program's by a relative error of at most 0.0003.
Values sent between devices are 32-bit elements; how exact they have to be, the bound alone decides.
No kernel may reach another device: no remote copies, remote signals or barrier semaphores. Data moves between devices by JAX's collectives and lax.ppermute only.
A program may use at most 64 MiB of HBM per device.

```python
import jax
import jax.numpy as jnp
from jax import lax

FRAMES = 2048
LEVELS = 4
VOXELS = 65536
N_VOX = 32


def tissue_class(count):
    return jnp.arange(count, dtype=jnp.int32) // 64 % 3


def draw_series(key, part):
    keys = jax.random.split(jax.random.fold_in(key, 11), 5)
    regions = VOXELS // 64
    noise = jax.random.normal(keys[0], (FRAMES, VOXELS), jnp.float32)
    courses = jax.random.normal(keys[1], (FRAMES, regions), jnp.float32)
    loads = jax.random.uniform(keys[2], (VOXELS,), jnp.float32, 0.5, 1.5)
    common = jax.random.normal(keys[3], (FRAMES,), jnp.float32)
    class_courses = jax.random.normal(keys[4], (FRAMES, 3), jnp.float32)
    member = (tissue_class(VOXELS)[None, :] == jnp.arange(3, dtype=jnp.int32)[:, None]).astype(jnp.float32)
    own_course = jnp.dot(class_courses, member, precision=jax.lax.Precision.HIGHEST)
    regional = jnp.repeat(courses, 64, axis=1)
    mixed = noise + loads[None, :] * (0.8 * common[:, None] + 0.8 * regional + 0.8 * own_course)
    return jnp.clip(mixed, -40.0, 40.0)


def draw_tissue(key, part):
    keys = jax.random.split(jax.random.fold_in(key, 23), 1)
    base_regressors = jax.random.uniform(keys[0], (3, VOXELS), jnp.float32, 0.1, 1.0)
    place = jnp.arange(VOXELS, dtype=jnp.float32) / float(VOXELS - 1)
    member = tissue_class(VOXELS)[None, :] == jnp.arange(3, dtype=jnp.int32)[:, None]
    focus = jnp.where(member, 1.0, 0.15).astype(jnp.float32)
    ramp = 1.0 + 2.0 * place
    return base_regressors * ramp[None, :] * focus


def set_ends(result, rng, smallest, largest):
    shape = result.shape
    index_at = [jax.random.randint(jax.random.fold_in(rng, axis), (), 0, shape[axis]) for axis in range(len(shape))]
    result = result.at[tuple(index_at)].set(smallest)
    longest = shape.index(max(shape))
    index_at[longest] = (index_at[longest] + 1) % shape[longest]
    return result.at[tuple(index_at)].set(largest)


def block_scale(key, dims, shards, smallest, largest):
    gain = 1.0
    for axis_at, shards_of in shards:
        steps = jax.random.uniform(jax.random.fold_in(jax.random.fold_in(key, 6), axis_at), (shards_of,), jnp.float32, smallest / len(shards), largest / len(shards))
        gain = gain * jnp.repeat(jnp.exp(steps), dims[axis_at] // shards_of).reshape((-1,) + (1,) * (len(dims) - 1 - axis_at))
    return gain


def normal_values(rng, dims, scale, most, shards=(), held_as=jnp.bfloat16):
    result = jax.random.normal(rng, dims, jnp.float32) * scale
    if len(shards) > 0:
        result = block_scale(rng, dims, shards, -0.22, 0.18) * result
    return jnp.clip(result, min=-most, max=most).astype(held_as)


def setup_inputs(seed: int = 0) -> dict:
    streams_of = jax.random.split(jax.random.key(seed), 5)
    series = draw_series(jax.random.fold_in(streams_of[4], 71), 0)
    spikes = set_ends(jax.random.randint(streams_of[1], (FRAMES, VOXELS), 0, 16), jax.random.fold_in(streams_of[1], 1), 0, 15).astype(jnp.int32)
    motion = normal_values(streams_of[2], (FRAMES, 6), 1.0, 5.0, ((0, 16),), jnp.float32)
    tissue = draw_tissue(jax.random.fold_in(streams_of[4], 71), 0)
    return {"series": series, "spikes": spikes, "motion": motion, "tissue": tissue}


def precise_product(left, right):
    return jnp.dot(left.astype(jnp.float32), right.astype(jnp.float32), precision=lax.Precision.HIGHEST, preferred_element_type=jnp.float32)

def despike(voxel_block, flags):
    approx = voxel_block
    kept_list = []
    for level in range(LEVELS):
        shift_rows = 2 ** level
        keep = 1.0 - (flags // 2 ** level % 2).astype(jnp.float32)
        lagged = jnp.roll(approx, shift_rows, axis=0)
        detail = (approx - lagged) * 0.5
        kept_list.append(detail * keep)
        approx = (approx + lagged) * 0.5
    for level in range(LEVELS - 1, -1, -1):
        shift_rows = 2 ** level
        kept = kept_list[level]
        lead_approx = jnp.roll(approx, -shift_rows, axis=0)
        lead_kept = jnp.roll(kept, -shift_rows, axis=0)
        approx = (approx + lead_approx) * 0.5 + (kept - lead_kept) * 0.5
    return approx

def assemble_nuisance_matrix(motion, voxel_signals, previous_frames):
    base_regressors = jnp.concatenate([motion, voxel_signals], axis=1)
    before = jnp.concatenate([previous_frames, base_regressors[:-1]], axis=0)
    temporal_derivative = base_regressors - before
    return jnp.concatenate([base_regressors, temporal_derivative, base_regressors * base_regressors, temporal_derivative * temporal_derivative], axis=1)

def reference(series, spikes, motion, tissue):
    frames = series.shape[0]
    width = series.shape[1] // N_VOX

    def first_pass(index, carry):
        store, numer = carry
        start = jnp.asarray(index).astype(jnp.int32) * width
        voxel_block = lax.dynamic_slice_in_dim(series, start, width, 1)
        flags = lax.dynamic_slice_in_dim(spikes, start, width, 1)
        weights = lax.dynamic_slice_in_dim(tissue, start, width, 1)
        clean_block = despike(voxel_block, flags)
        numer = numer + precise_product(clean_block, weights.T)
        store = lax.dynamic_update_slice_in_dim(store, clean_block, start, 1)
        return (store, numer)
    store0 = jnp.zeros(series.shape, jnp.float32)
    numer0 = jnp.zeros((frames, 3), jnp.float32)
    spike_free_series, numer = lax.fori_loop(0, N_VOX, first_pass, (store0, numer0))
    voxel_signals = numer / float(VOXELS)
    nuisance_matrix = assemble_nuisance_matrix(motion, voxel_signals, jnp.zeros((1, 9), jnp.float32))
    gram_matrix = precise_product(nuisance_matrix.T, nuisance_matrix)
    factor = jnp.linalg.cholesky(gram_matrix)

    def second_pass(index, store):
        start = jnp.asarray(index).astype(jnp.int32) * width
        voxel_block = lax.dynamic_slice_in_dim(spike_free_series, start, width, 1)
        cross_products = precise_product(nuisance_matrix.T, voxel_block)
        beta_estimates = jax.scipy.linalg.cho_solve((factor, True), cross_products)
        residual_output = voxel_block - precise_product(nuisance_matrix, beta_estimates)
        return lax.dynamic_update_slice_in_dim(store, residual_output, start, 1)
    return lax.fori_loop(0, N_VOX, second_pass, jnp.zeros(series.shape, jnp.float32))
```

```python
import jax
import jax.numpy as jnp
from jax import lax
from jax.sharding import PartitionSpec as P

LEVELS = 4
HALO = 16


def from_behind(block, axis, distance):
    devices = range(lax.axis_size(axis))
    route = [((i - distance) % len(devices), i) for i in devices]
    return lax.ppermute(block, axis, route)


def precise_product(left, right):
    return jnp.dot(left, right, precision=lax.Precision.HIGHEST, preferred_element_type=jnp.float32)


def keep_level(spikes, level):
    return 1.0 - (spikes // 2**level % 2).astype(jnp.float32)


def despike_window(window, flags):
    approx = window
    kept_list = []
    for level in range(LEVELS):
        shift_rows = 2**level
        lagged = jnp.roll(approx, shift_rows, axis=0)
        detail = (approx - lagged) * 0.5
        kept_list.append(detail * keep_level(flags, level))
        approx = (approx + lagged) * 0.5
    for level in range(LEVELS - 1, -1, -1):
        shift_rows = 2**level
        kept = kept_list[level]
        lead_approx = jnp.roll(approx, -shift_rows, axis=0)
        lead_kept = jnp.roll(kept, -shift_rows, axis=0)
        approx = (approx + lead_approx) * 0.5 + (kept - lead_kept) * 0.5
    return approx


def sum_over_vox(block):
    n = lax.axis_size("vox")
    copies = jnp.broadcast_to(block, (n,) + block.shape)
    return lax.all_to_all(copies, "vox", 0, 0, tiled=False).sum(axis=0)


def sum_over_tm(block):
    n = lax.axis_size("tm")
    rows, cols = block.shape
    parts = block.reshape(rows, n, cols // n).transpose(1, 0, 2)
    owned = lax.all_to_all(parts, "tm", 0, 0, tiled=False).sum(axis=0)
    copies = jnp.broadcast_to(owned, (n,) + owned.shape)
    gathered = lax.all_to_all(copies, "tm", 0, 0, tiled=False)
    return gathered.transpose(1, 0, 2).reshape(rows, cols)


def local(series, spikes, motion, tissue):
    frames = series.shape[0]
    flags = spikes.astype(jnp.float32)
    tail = jnp.stack([series[frames - HALO :], flags[frames - HALO :]])
    head = jnp.stack([series[:HALO], flags[:HALO]])
    before = from_behind(tail, "tm", 1)
    after = from_behind(head, "tm", -1)
    motion_before = from_behind(motion[frames - 1 :], "tm", 1)
    window = jnp.concatenate([before[0], series, after[0]], axis=0)
    window_flags = jnp.concatenate([before[1], flags, after[1]], axis=0).astype(jnp.int32)
    despiked_window = despike_window(window, window_flags)
    spike_free_series = despiked_window[HALO : HALO + frames]

    rows = despiked_window[HALO - 8 : HALO + frames]
    numer = sum_over_vox(precise_product(rows, tissue.T))
    voxel_signals = numer / float(tissue.shape[1] * lax.axis_size("vox"))

    first = lax.axis_index("tm") == 0
    base_before = jnp.concatenate([motion_before, voxel_signals[7:8]], axis=1)
    base_before = jnp.where(first, jnp.zeros_like(base_before), base_before)
    base_regressors = jnp.concatenate([motion, voxel_signals[8:]], axis=1)
    previous = jnp.concatenate([base_before, base_regressors[:-1]], axis=0)
    temporal_derivative = base_regressors - previous
    nuisance_matrix = jnp.concatenate(
        [
            base_regressors,
            temporal_derivative,
            base_regressors * base_regressors,
            temporal_derivative * temporal_derivative,
        ],
        axis=1,
    )
    terms = nuisance_matrix.shape[1]
    voxels = series.shape[1]
    gram_matrix = precise_product(nuisance_matrix.T, nuisance_matrix)
    cross_products = precise_product(nuisance_matrix.T, spike_free_series)
    gram_rows = -(-terms * terms // voxels)
    gram_flat = jnp.pad(gram_matrix.reshape(terms * terms), (0, gram_rows * voxels - terms * terms))
    packed = jnp.concatenate([cross_products, gram_flat.reshape(gram_rows, voxels)], axis=0)
    summed = sum_over_tm(packed)
    cross_products = summed[:terms]
    gram_matrix = summed[terms:].reshape(-1)[: terms * terms].reshape(terms, terms)
    factor = jnp.linalg.cholesky(gram_matrix)
    beta_estimates = jax.scipy.linalg.cho_solve((factor, True), cross_products)
    return spike_free_series - precise_product(nuisance_matrix, beta_estimates)


def solution(mesh):
    return jax.shard_map(
        local,
        mesh=mesh,
        in_specs=(P("tm", "vox"), P("tm", "vox"), P("tm", None), P(None, "vox")),
        out_specs=P("tm", "vox"),
        check_vma=False,
    )
```

```python
import jax
import jax.numpy as jnp
from jax import lax
from jax.sharding import PartitionSpec as P

LEVELS = 4
HALO = 16


def from_behind(block, axis, distance):
    devices = range(lax.axis_size(axis))
    route = [((i - distance) % len(devices), i) for i in devices]
    return lax.ppermute(block, axis, route)


def precise_product(left, right):
    return jnp.dot(left, right, precision=lax.Precision.HIGHEST, preferred_element_type=jnp.float32)


def keep_level(spikes, level):
    return 1.0 - (spikes // 2**level % 2).astype(jnp.float32)


def despike_window(window, flags):
    approx = window
    kept_list = []
    for level in range(LEVELS):
        shift_rows = 2**level
        lagged = jnp.roll(approx, shift_rows, axis=0)
        detail = (approx - lagged) * 0.5
        kept_list.append(detail * keep_level(flags, level))
        approx = (approx + lagged) * 0.5
    for level in range(LEVELS - 1, -1, -1):
        shift_rows = 2**level
        kept = kept_list[level]
        lead_approx = jnp.roll(approx, -shift_rows, axis=0)
        lead_kept = jnp.roll(kept, -shift_rows, axis=0)
        approx = (approx + lead_approx) * 0.5 + (kept - lead_kept) * 0.5
    return approx


def sum_over_vox(block):
    n = lax.axis_size("vox")
    copies = jnp.broadcast_to(block, (n,) + block.shape)
    return lax.all_to_all(copies, "vox", 0, 0, tiled=False).sum(axis=0)


def sum_over_tm(block):
    n = lax.axis_size("tm")
    rows, cols = block.shape
    parts = block.reshape(rows, n, cols // n).transpose(1, 0, 2)
    owned = lax.all_to_all(parts, "tm", 0, 0, tiled=False).sum(axis=0)
    copies = jnp.broadcast_to(owned, (n,) + owned.shape)
    gathered = lax.all_to_all(copies, "tm", 0, 0, tiled=False)
    return gathered.transpose(1, 0, 2).reshape(rows, cols)


def local(series, spikes, motion, tissue):
    frames = series.shape[0]
    tail = jnp.stack([series[frames - HALO :], spikes[frames - HALO :].astype(jnp.float32)])
    head = jnp.stack([series[:HALO], spikes[:HALO].astype(jnp.float32)])
    before = from_behind(tail, "tm", 1)
    after = from_behind(head, "tm", -1)
    motion_before = from_behind(motion[frames - 1 :], "tm", 1)
    inner = despike_window(series, spikes)
    edge = 2 * HALO
    head_window = despike_window(
        jnp.concatenate([before[0], series[:edge]], axis=0),
        jnp.concatenate([before[1].astype(jnp.int32), spikes[:edge]], axis=0),
    )
    tail_window = despike_window(
        jnp.concatenate([series[frames - edge :], after[0]], axis=0),
        jnp.concatenate([spikes[frames - edge :], after[1].astype(jnp.int32)], axis=0),
    )
    spike_free_series = jnp.concatenate(
        [head_window[HALO:edge], inner[HALO : frames - HALO], tail_window[HALO:edge]], axis=0
    )
    despiked_window = jnp.concatenate([head_window[:HALO], spike_free_series], axis=0)

    rows = despiked_window[HALO - 8 : HALO + frames]
    numer = sum_over_vox(precise_product(rows, tissue.T))
    voxel_signals = numer / float(tissue.shape[1] * lax.axis_size("vox"))

    first = lax.axis_index("tm") == 0
    base_before = jnp.concatenate([motion_before, voxel_signals[7:8]], axis=1)
    base_before = jnp.where(first, jnp.zeros_like(base_before), base_before)
    base_regressors = jnp.concatenate([motion, voxel_signals[8:]], axis=1)
    previous = jnp.concatenate([base_before, base_regressors[:-1]], axis=0)
    temporal_derivative = base_regressors - previous
    nuisance_matrix = jnp.concatenate(
        [
            base_regressors,
            temporal_derivative,
            base_regressors * base_regressors,
            temporal_derivative * temporal_derivative,
        ],
        axis=1,
    )
    terms = nuisance_matrix.shape[1]
    voxels = series.shape[1]
    gram_matrix = precise_product(nuisance_matrix.T, nuisance_matrix)
    cross_products = precise_product(nuisance_matrix.T, spike_free_series)
    gram_rows = -(-terms * terms // voxels)
    gram_flat = jnp.pad(gram_matrix.reshape(terms * terms), (0, gram_rows * voxels - terms * terms))
    packed = jnp.concatenate([cross_products, gram_flat.reshape(gram_rows, voxels)], axis=0)
    summed = sum_over_tm(packed)
    cross_products = summed[:terms]
    gram_matrix = summed[terms:].reshape(-1)[: terms * terms].reshape(terms, terms)
    factor = jnp.linalg.cholesky(gram_matrix)
    beta_estimates = jax.scipy.linalg.cho_solve((factor, True), cross_products)
    return spike_free_series - precise_product(nuisance_matrix, beta_estimates)


def solution(mesh):
    return jax.shard_map(
        local,
        mesh=mesh,
        in_specs=(P("tm", "vox"), P("tm", "vox"), P("tm", None), P(None, "vox")),
        out_specs=P("tm", "vox"),
        check_vma=False,
    )
```

```python
import jax
import jax.numpy as jnp
from jax import lax
from jax.sharding import PartitionSpec as P

LEVELS = 4
HALO = 16


def from_behind(block, axis, distance):
    devices = range(lax.axis_size(axis))
    route = [((i - distance) % len(devices), i) for i in devices]
    return lax.ppermute(block, axis, route)


def precise_product(left, right):
    return jnp.dot(left, right, precision=lax.Precision.HIGHEST, preferred_element_type=jnp.float32)


def keep_level(spikes, level):
    return 1.0 - (spikes // 2**level % 2).astype(jnp.float32)


def despike_window(window, flags):
    approx = window
    kept_list = []
    for level in range(LEVELS):
        shift_rows = 2**level
        lagged = jnp.roll(approx, shift_rows, axis=0)
        detail = (approx - lagged) * 0.5
        kept_list.append(detail * keep_level(flags, level))
        approx = (approx + lagged) * 0.5
    for level in range(LEVELS - 1, -1, -1):
        shift_rows = 2**level
        kept = kept_list[level]
        lead_approx = jnp.roll(approx, -shift_rows, axis=0)
        lead_kept = jnp.roll(kept, -shift_rows, axis=0)
        approx = (approx + lead_approx) * 0.5 + (kept - lead_kept) * 0.5
    return approx


def sum_over_vox(block):
    n = lax.axis_size("vox")
    copies = jnp.broadcast_to(block, (n,) + block.shape)
    return lax.all_to_all(copies, "vox", 0, 0, tiled=False).sum(axis=0)


def sum_over_tm(block, pieces=4):
    n = lax.axis_size("tm")
    rows, cols = block.shape
    width = cols // n
    parts = block.reshape(rows, n, width).transpose(1, 0, 2)
    step = width // pieces
    owned = [
        lax.all_to_all(parts[:, :, q * step : (q + 1) * step], "tm", 0, 0, tiled=False).sum(axis=0)
        for q in range(pieces)
    ]
    gathered = [
        lax.all_to_all(jnp.broadcast_to(o, (n,) + o.shape), "tm", 0, 0, tiled=False) for o in owned
    ]
    return jnp.concatenate(gathered, axis=2).transpose(1, 0, 2).reshape(rows, cols)


def local(series, spikes, motion, tissue):
    frames = series.shape[0]
    tail = jnp.stack([series[frames - HALO :], spikes[frames - HALO :].astype(jnp.float32)])
    head = jnp.stack([series[:HALO], spikes[:HALO].astype(jnp.float32)])
    before = from_behind(tail, "tm", 1)
    after = from_behind(head, "tm", -1)
    motion_before = from_behind(motion[frames - 1 :], "tm", 1)
    inner = despike_window(series, spikes)
    edge = 2 * HALO
    head_window = despike_window(
        jnp.concatenate([before[0], series[:edge]], axis=0),
        jnp.concatenate([before[1].astype(jnp.int32), spikes[:edge]], axis=0),
    )
    tail_window = despike_window(
        jnp.concatenate([series[frames - edge :], after[0]], axis=0),
        jnp.concatenate([spikes[frames - edge :], after[1].astype(jnp.int32)], axis=0),
    )
    spike_free_series = jnp.concatenate(
        [head_window[HALO:edge], inner[HALO : frames - HALO], tail_window[HALO:edge]], axis=0
    )
    despiked_window = jnp.concatenate([head_window[:HALO], spike_free_series], axis=0)

    rows = despiked_window[HALO - 8 : HALO + frames]
    numer = sum_over_vox(precise_product(rows, tissue.T))
    voxel_signals = numer / float(tissue.shape[1] * lax.axis_size("vox"))

    first = lax.axis_index("tm") == 0
    base_before = jnp.concatenate([motion_before, voxel_signals[7:8]], axis=1)
    base_before = jnp.where(first, jnp.zeros_like(base_before), base_before)
    base_regressors = jnp.concatenate([motion, voxel_signals[8:]], axis=1)
    previous = jnp.concatenate([base_before, base_regressors[:-1]], axis=0)
    temporal_derivative = base_regressors - previous
    nuisance_matrix = jnp.concatenate(
        [
            base_regressors,
            temporal_derivative,
            base_regressors * base_regressors,
            temporal_derivative * temporal_derivative,
        ],
        axis=1,
    )
    terms = nuisance_matrix.shape[1]
    voxels = series.shape[1]
    gram_matrix = precise_product(nuisance_matrix.T, nuisance_matrix)
    cross_products = precise_product(nuisance_matrix.T, spike_free_series)
    gram_rows = -(-terms * terms // voxels)
    gram_flat = jnp.pad(gram_matrix.reshape(terms * terms), (0, gram_rows * voxels - terms * terms))
    packed = jnp.concatenate([cross_products, gram_flat.reshape(gram_rows, voxels)], axis=0)
    summed = sum_over_tm(packed)
    cross_products = summed[:terms]
    gram_matrix = summed[terms:].reshape(-1)[: terms * terms].reshape(terms, terms)
    factor = jnp.linalg.cholesky(gram_matrix)
    beta_estimates = jax.scipy.linalg.cho_solve((factor, True), cross_products)
    return spike_free_series - precise_product(nuisance_matrix, beta_estimates)


def solution(mesh):
    return jax.shard_map(
        local,
        mesh=mesh,
        in_specs=(P("tm", "vox"), P("tm", "vox"), P("tm", None), P(None, "vox")),
        out_specs=P("tm", "vox"),
        check_vma=False,
    )
```

```python
import jax
import jax.numpy as jnp
from jax import lax
from jax.sharding import PartitionSpec as P

LEVELS = 4
HALO = 16


def from_behind(block, axis, distance):
    devices = range(lax.axis_size(axis))
    route = [((i - distance) % len(devices), i) for i in devices]
    return lax.ppermute(block, axis, route)


def precise_product(left, right):
    return jnp.dot(left, right, precision=lax.Precision.HIGHEST, preferred_element_type=jnp.float32)


def keep_level(spikes, level):
    return 1.0 - (spikes // 2**level % 2).astype(jnp.float32)


def despike_trimmed(window, flags):
    length = window.shape[0]
    approx = window
    start = 0
    kept_list = []
    for level in range(LEVELS):
        shift_rows = 2**level
        current, lagged = approx[shift_rows:], approx[:-shift_rows]
        start += shift_rows
        keep = keep_level(flags[start:], level)
        kept_list.append((start, (current - lagged) * 0.5 * keep))
        approx = (current + lagged) * 0.5
    for level in range(LEVELS - 1, -1, -1):
        shift_rows = 2**level
        kept_start, kept = kept_list[level]
        kept = kept[start - kept_start : start - kept_start + approx.shape[0]]
        approx = (approx[:-shift_rows] + approx[shift_rows:]) * 0.5 + (kept[:-shift_rows] - kept[shift_rows:]) * 0.5
    return approx


def sum_over_vox(block):
    n = lax.axis_size("vox")
    copies = jnp.broadcast_to(block, (n,) + block.shape)
    return lax.all_to_all(copies, "vox", 0, 0, tiled=False).sum(axis=0)


def sum_over_tm(block):
    n = lax.axis_size("tm")
    rows, cols = block.shape
    parts = block.reshape(rows, n, cols // n).transpose(1, 0, 2)
    owned = lax.all_to_all(parts, "tm", 0, 0, tiled=False).sum(axis=0)
    copies = jnp.broadcast_to(owned, (n,) + owned.shape)
    gathered = lax.all_to_all(copies, "tm", 0, 0, tiled=False)
    return gathered.transpose(1, 0, 2).reshape(rows, cols)


def local(series, spikes, motion, tissue):
    frames = series.shape[0]
    voxels = series.shape[1]
    motion_row = jnp.pad(motion[frames - 1 :], ((0, 7), (0, voxels - motion.shape[1])))
    tail = jnp.concatenate([series[frames - HALO :], spikes[frames - HALO :].astype(jnp.float32), motion_row], axis=0)
    head = jnp.concatenate([series[:HALO], spikes[:HALO].astype(jnp.float32)], axis=0)
    before = from_behind(tail, "tm", 1)
    after = from_behind(head, "tm", -1)
    motion_before = before[2 * HALO : 2 * HALO + 1, : motion.shape[1]]
    inner = despike_trimmed(series, spikes)
    edge = 2 * HALO
    head_window = despike_trimmed(
        jnp.concatenate([before[:HALO], series[:edge]], axis=0),
        jnp.concatenate([before[HALO : 2 * HALO].astype(jnp.int32), spikes[:edge]], axis=0),
    )
    tail_window = despike_trimmed(
        jnp.concatenate([series[frames - edge :], after[:HALO]], axis=0),
        jnp.concatenate([spikes[frames - edge :], after[HALO:].astype(jnp.int32)], axis=0),
    )
    spike_free_series = jnp.concatenate([head_window[1 : HALO + 1], inner[1 : frames - 31], tail_window[1 : HALO + 1]], axis=0)
    despiked_window = jnp.concatenate([jnp.zeros((HALO - 1, voxels), jnp.float32), head_window[:1], spike_free_series], axis=0)

    rows = despiked_window[HALO - 8 : HALO + frames]
    numer = sum_over_vox(precise_product(rows, tissue.T))
    voxel_signals = numer / float(tissue.shape[1] * lax.axis_size("vox"))

    first = lax.axis_index("tm") == 0
    base_before = jnp.concatenate([motion_before, voxel_signals[7:8]], axis=1)
    base_before = jnp.where(first, jnp.zeros_like(base_before), base_before)
    base_regressors = jnp.concatenate([motion, voxel_signals[8:]], axis=1)
    previous = jnp.concatenate([base_before, base_regressors[:-1]], axis=0)
    temporal_derivative = base_regressors - previous
    nuisance_matrix = jnp.concatenate(
        [
            base_regressors,
            temporal_derivative,
            base_regressors * base_regressors,
            temporal_derivative * temporal_derivative,
        ],
        axis=1,
    )
    terms = nuisance_matrix.shape[1]
    gram_matrix = precise_product(nuisance_matrix.T, nuisance_matrix)
    cross_products = precise_product(nuisance_matrix.T, spike_free_series)
    gram_rows = -(-terms * terms // voxels)
    gram_flat = jnp.pad(gram_matrix.reshape(terms * terms), (0, gram_rows * voxels - terms * terms))
    packed = jnp.concatenate([cross_products, gram_flat.reshape(gram_rows, voxels)], axis=0)
    summed = sum_over_tm(packed)
    cross_products = summed[:terms]
    gram_matrix = summed[terms:].reshape(-1)[: terms * terms].reshape(terms, terms)
    factor = jnp.linalg.cholesky(gram_matrix)
    beta_estimates = jax.scipy.linalg.cho_solve((factor, True), cross_products)
    return spike_free_series - precise_product(nuisance_matrix, beta_estimates)


def solution(mesh):
    return jax.shard_map(
        local,
        mesh=mesh,
        in_specs=(P("tm", "vox"), P("tm", "vox"), P("tm", None), P(None, "vox")),
        out_specs=P("tm", "vox"),
        check_vma=False,
    )
```

```python
import jax
import jax.numpy as jnp
from jax import lax
from jax.sharding import PartitionSpec as P

LEVELS = 4
HALO = 16


def from_behind(block, axis, distance):
    devices = range(lax.axis_size(axis))
    route = [((i - distance) % len(devices), i) for i in devices]
    return lax.ppermute(block, axis, route)


def precise_product(left, right):
    return jnp.dot(left, right, precision=lax.Precision.HIGHEST, preferred_element_type=jnp.float32)


def keep_level(spikes, level):
    return 1.0 - (spikes // 2**level % 2).astype(jnp.float32)


def despike_trimmed(window, flags):
    length = window.shape[0]
    approx = window
    start = 0
    kept_list = []
    for level in range(LEVELS):
        shift_rows = 2**level
        current, lagged = approx[shift_rows:], approx[:-shift_rows]
        start += shift_rows
        keep = keep_level(flags[start:], level)
        kept_list.append((start, (current - lagged) * 0.5 * keep))
        approx = (current + lagged) * 0.5
    for level in range(LEVELS - 1, -1, -1):
        shift_rows = 2**level
        kept_start, kept = kept_list[level]
        kept = kept[start - kept_start : start - kept_start + approx.shape[0]]
        approx = (approx[:-shift_rows] + approx[shift_rows:]) * 0.5 + (kept[:-shift_rows] - kept[shift_rows:]) * 0.5
    return approx


def sum_over_vox(block):
    n = lax.axis_size("vox")
    copies = jnp.broadcast_to(block, (n,) + block.shape)
    return lax.all_to_all(copies, "vox", 0, 0, tiled=False).sum(axis=0)


def sum_over_tm(block):
    n = lax.axis_size("tm")
    rows, cols = block.shape
    parts = block.reshape(rows, n, cols // n).transpose(1, 0, 2)
    owned = lax.all_to_all(parts, "tm", 0, 0, tiled=False).sum(axis=0)
    copies = jnp.broadcast_to(owned, (n,) + owned.shape)
    gathered = lax.all_to_all(copies, "tm", 0, 0, tiled=False)
    return gathered.transpose(1, 0, 2).reshape(rows, cols)


def local(series, spikes, motion, tissue):
    frames = series.shape[0]
    voxels = series.shape[1]
    motion_row = jnp.pad(motion[frames - 1 :], ((0, 7), (0, voxels - motion.shape[1])))
    tail = jnp.concatenate([series[frames - HALO :], spikes[frames - HALO :].astype(jnp.float32), motion_row], axis=0)
    head = jnp.concatenate([series[:HALO], spikes[:HALO].astype(jnp.float32)], axis=0)
    before = from_behind(tail, "tm", 1)
    after = from_behind(head, "tm", -1)
    motion_before = before[2 * HALO : 2 * HALO + 1, : motion.shape[1]]
    inner = despike_trimmed(series, spikes)
    edge = 2 * HALO
    head_window = despike_trimmed(
        jnp.concatenate([before[:HALO], series[:edge]], axis=0),
        jnp.concatenate([before[HALO : 2 * HALO].astype(jnp.int32), spikes[:edge]], axis=0),
    )
    tail_window = despike_trimmed(
        jnp.concatenate([series[frames - edge :], after[:HALO]], axis=0),
        jnp.concatenate([spikes[frames - edge :], after[HALO:].astype(jnp.int32)], axis=0),
    )
    spike_free_series = jnp.concatenate([head_window[1 : HALO + 1], inner[1 : frames - 31], tail_window[1 : HALO + 1]], axis=0)
    despiked_window = jnp.concatenate([jnp.zeros((HALO - 1, voxels), jnp.float32), head_window[:1], spike_free_series], axis=0)

    rows = despiked_window[HALO - 8 : HALO + frames]
    numer = sum_over_vox(precise_product(rows, tissue.T))
    voxel_signals = numer / float(tissue.shape[1] * lax.axis_size("vox"))

    first = lax.axis_index("tm") == 0
    base_before = jnp.concatenate([motion_before, voxel_signals[7:8]], axis=1)
    base_before = jnp.where(first, jnp.zeros_like(base_before), base_before)
    base_regressors = jnp.concatenate([motion, voxel_signals[8:]], axis=1)
    previous = jnp.concatenate([base_before, base_regressors[:-1]], axis=0)
    temporal_derivative = base_regressors - previous
    nuisance_matrix = jnp.concatenate(
        [
            base_regressors,
            temporal_derivative,
            base_regressors * base_regressors,
            temporal_derivative * temporal_derivative,
        ],
        axis=1,
    )
    terms = nuisance_matrix.shape[1]
    gram_matrix = precise_product(nuisance_matrix.T, nuisance_matrix)
    cross_products = precise_product(nuisance_matrix.T, spike_free_series)
    gram_rows = -(-terms * terms // voxels)
    gram_flat = jnp.pad(gram_matrix.reshape(terms * terms), (0, gram_rows * voxels - terms * terms))
    packed = jnp.concatenate([cross_products, gram_flat.reshape(gram_rows, voxels)], axis=0)
    summed = sum_over_tm(packed)
    cross_products = summed[:terms]
    gram_matrix = summed[terms:].reshape(-1)[: terms * terms].reshape(terms, terms)
    factor = jnp.linalg.cholesky(gram_matrix)
    weights = jax.scipy.linalg.cho_solve((factor, True), nuisance_matrix.T)
    return spike_free_series - precise_product(weights.T, cross_products)


def solution(mesh):
    return jax.shard_map(
        local,
        mesh=mesh,
        in_specs=(P("tm", "vox"), P("tm", "vox"), P("tm", None), P(None, "vox")),
        out_specs=P("tm", "vox"),
        check_vma=False,
    )
```

```python
import jax
import jax.numpy as jnp
from jax import lax
from jax.sharding import PartitionSpec as P

LEVELS = 4
HALO = 16


def from_behind(block, axis, distance):
    devices = range(lax.axis_size(axis))
    route = [((i - distance) % len(devices), i) for i in devices]
    return lax.ppermute(block, axis, route)


def precise_product(left, right):
    return jnp.dot(left, right, precision=lax.Precision.HIGHEST, preferred_element_type=jnp.float32)


def keep_level(spikes, level):
    return 1.0 - (spikes // 2**level % 2).astype(jnp.float32)


def despike_trimmed(window, flags):
    length = window.shape[0]
    approx = window
    start = 0
    kept_list = []
    for level in range(LEVELS):
        shift_rows = 2**level
        current, lagged = approx[shift_rows:], approx[:-shift_rows]
        start += shift_rows
        keep = keep_level(flags[start:], level)
        kept_list.append((start, (current - lagged) * 0.5 * keep))
        approx = (current + lagged) * 0.5
    for level in range(LEVELS - 1, -1, -1):
        shift_rows = 2**level
        kept_start, kept = kept_list[level]
        kept = kept[start - kept_start : start - kept_start + approx.shape[0]]
        approx = (approx[:-shift_rows] + approx[shift_rows:]) * 0.5 + (kept[:-shift_rows] - kept[shift_rows:]) * 0.5
    return approx


def sum_over_vox(block):
    n = lax.axis_size("vox")
    copies = jnp.broadcast_to(block, (n,) + block.shape)
    return lax.all_to_all(copies, "vox", 0, 0, tiled=False).sum(axis=0)


def scatter_over_tm(block):
    n = lax.axis_size("tm")
    rows, cols = block.shape
    parts = block.reshape(rows, n, cols // n).transpose(1, 0, 2)
    return lax.all_to_all(parts, "tm", 0, 0, tiled=False).sum(axis=0)


def gather_over_tm(owned):
    n = lax.axis_size("tm")
    rows, width = owned.shape
    copies = jnp.broadcast_to(owned, (n,) + owned.shape)
    gathered = lax.all_to_all(copies, "tm", 0, 0, tiled=False)
    return gathered.transpose(1, 0, 2).reshape(rows, n * width)


def with_flat(block, small, voxels):
    size = small.size
    rows = -(-size // voxels)
    flat = jnp.pad(small.reshape(size), (0, rows * voxels - size))
    return jnp.concatenate([block, flat.reshape(rows, voxels)], axis=0)


def flat_part(summed, first_row, shape):
    size = shape[0] * shape[1]
    return summed[first_row:].reshape(-1)[:size].reshape(shape)


def local(series, spikes, motion, tissue):
    frames = series.shape[0]
    voxels = series.shape[1]
    motion_row = jnp.pad(motion[frames - 1 :], ((0, 7), (0, voxels - motion.shape[1])))
    tail = jnp.concatenate([series[frames - HALO :], spikes[frames - HALO :].astype(jnp.float32), motion_row], axis=0)
    head = jnp.concatenate([series[:HALO], spikes[:HALO].astype(jnp.float32)], axis=0)
    before = from_behind(tail, "tm", 1)
    after = from_behind(head, "tm", -1)
    motion_before = before[2 * HALO : 2 * HALO + 1, : motion.shape[1]]
    inner = despike_trimmed(series, spikes)
    edge = 2 * HALO
    head_window = despike_trimmed(
        jnp.concatenate([before[:HALO], series[:edge]], axis=0),
        jnp.concatenate([before[HALO : 2 * HALO].astype(jnp.int32), spikes[:edge]], axis=0),
    )
    tail_window = despike_trimmed(
        jnp.concatenate([series[frames - edge :], after[:HALO]], axis=0),
        jnp.concatenate([spikes[frames - edge :], after[HALO:].astype(jnp.int32)], axis=0),
    )
    spike_free_series = jnp.concatenate([head_window[1 : HALO + 1], inner[1 : frames - 31], tail_window[1 : HALO + 1]], axis=0)
    despiked_window = jnp.concatenate([jnp.zeros((HALO - 1, voxels), jnp.float32), head_window[:1], spike_free_series], axis=0)

    rows = despiked_window[HALO - 8 : HALO + frames]
    first = lax.axis_index("tm") == 0
    motion_before = jnp.where(first, jnp.zeros_like(motion_before), motion_before)
    motion_derivative = motion - jnp.concatenate([motion_before, motion[:-1]], axis=0)
    motion_terms = jnp.concatenate(
        [motion, motion_derivative, motion * motion, motion_derivative * motion_derivative], axis=1
    )
    motion_cross = precise_product(motion_terms.T, spike_free_series)
    motion_gram = precise_product(motion_terms.T, motion_terms)
    owned_motion = scatter_over_tm(with_flat(motion_cross, motion_gram, voxels))

    numer = sum_over_vox(precise_product(rows, tissue.T))
    voxel_signals = numer / float(tissue.shape[1] * lax.axis_size("vox"))
    signals_before = jnp.where(first, jnp.zeros_like(voxel_signals[7:8]), voxel_signals[7:8])
    signals = voxel_signals[8:]
    signal_derivative = signals - jnp.concatenate([signals_before, signals[:-1]], axis=0)
    signal_terms = jnp.concatenate(
        [signals, signal_derivative, signals * signals, signal_derivative * signal_derivative], axis=1
    )
    nuisance_matrix = jnp.concatenate([motion_terms, signal_terms], axis=1)
    signal_cross = precise_product(signal_terms.T, spike_free_series)
    signal_gram = precise_product(signal_terms.T, nuisance_matrix)
    owned_signal = scatter_over_tm(with_flat(signal_cross, signal_gram, voxels))

    moving, signaled = motion_terms.shape[1], signal_terms.shape[1]
    summed = gather_over_tm(jnp.concatenate([owned_motion, owned_signal], axis=0))
    split = owned_motion.shape[0]
    cross_products = jnp.concatenate([summed[:moving], summed[split : split + signaled]], axis=0)
    gram_mm = flat_part(summed, moving, (moving, moving))
    gram_s = flat_part(summed, split + signaled, (signaled, moving + signaled))
    gram_matrix = jnp.concatenate([jnp.concatenate([gram_mm, gram_s[:, :moving].T], axis=1), gram_s], axis=0)
    factor = jnp.linalg.cholesky(gram_matrix)
    weights = jax.scipy.linalg.cho_solve((factor, True), nuisance_matrix.T)
    return spike_free_series - precise_product(weights.T, cross_products)


def solution(mesh):
    return jax.shard_map(
        local,
        mesh=mesh,
        in_specs=(P("tm", "vox"), P("tm", "vox"), P("tm", None), P(None, "vox")),
        out_specs=P("tm", "vox"),
        check_vma=False,
    )
```

```python
import jax
import jax.numpy as jnp
from jax import lax
from jax.sharding import PartitionSpec as P

LEVELS = 4
HALO = 16


def from_behind(block, axis, distance):
    devices = range(lax.axis_size(axis))
    route = [((i - distance) % len(devices), i) for i in devices]
    return lax.ppermute(block, axis, route)


def precise_product(left, right):
    return jnp.dot(left, right, precision=lax.Precision.HIGHEST, preferred_element_type=jnp.float32)


def keep_level(spikes, level):
    return 1.0 - (spikes // 2**level % 2).astype(jnp.float32)


def despike_trimmed(window, flags):
    length = window.shape[0]
    approx = window
    start = 0
    kept_list = []
    for level in range(LEVELS):
        shift_rows = 2**level
        current, lagged = approx[shift_rows:], approx[:-shift_rows]
        start += shift_rows
        keep = keep_level(flags[start:], level)
        kept_list.append((start, (current - lagged) * 0.5 * keep))
        approx = (current + lagged) * 0.5
    for level in range(LEVELS - 1, -1, -1):
        shift_rows = 2**level
        kept_start, kept = kept_list[level]
        kept = kept[start - kept_start : start - kept_start + approx.shape[0]]
        approx = (approx[:-shift_rows] + approx[shift_rows:]) * 0.5 + (kept[:-shift_rows] - kept[shift_rows:]) * 0.5
    return approx


def sum_over_vox(block):
    n = lax.axis_size("vox")
    copies = jnp.broadcast_to(block, (n,) + block.shape)
    return lax.all_to_all(copies, "vox", 0, 0, tiled=False).sum(axis=0)


def sum_over_tm(block):
    n = lax.axis_size("tm")
    rows, cols = block.shape
    parts = block.reshape(rows, n, cols // n).transpose(1, 0, 2)
    owned = lax.all_to_all(parts, "tm", 0, 0, tiled=False).sum(axis=0)
    copies = jnp.broadcast_to(owned, (n,) + owned.shape)
    gathered = lax.all_to_all(copies, "tm", 0, 0, tiled=False)
    return gathered.transpose(1, 0, 2).reshape(rows, cols)


def local(series, spikes, motion, tissue):
    frames = series.shape[0]
    voxels = series.shape[1]
    last_rows = jnp.concatenate(
        [spikes[frames - 1 :].astype(jnp.float32), jnp.pad(motion[frames - 1 :], ((0, 0), (0, voxels - motion.shape[1])))],
        axis=0,
    )
    tail = jnp.concatenate([series[frames - HALO :], jnp.pad(last_rows, ((0, 6), (0, 0)))], axis=0)
    head = jnp.concatenate([series[:HALO], spikes[:HALO].astype(jnp.float32)], axis=0)
    before = from_behind(tail, "tm", 1)
    after = from_behind(head, "tm", -1)
    motion_before = before[HALO + 1 : HALO + 2, : motion.shape[1]]
    flags_before = jnp.concatenate(
        [jnp.zeros((HALO - 1, voxels), jnp.int32), before[HALO : HALO + 1].astype(jnp.int32)], axis=0
    )
    inner = despike_trimmed(series, spikes)
    edge = 2 * HALO
    head_window = despike_trimmed(
        jnp.concatenate([before[:HALO], series[:edge]], axis=0),
        jnp.concatenate([flags_before, spikes[:edge]], axis=0),
    )
    tail_window = despike_trimmed(
        jnp.concatenate([series[frames - edge :], after[:HALO]], axis=0),
        jnp.concatenate([spikes[frames - edge :], after[HALO:].astype(jnp.int32)], axis=0),
    )
    spike_free_series = jnp.concatenate([head_window[1 : HALO + 1], inner[1 : frames - 31], tail_window[1 : HALO + 1]], axis=0)
    despiked_window = jnp.concatenate([jnp.zeros((HALO - 1, voxels), jnp.float32), head_window[:1], spike_free_series], axis=0)

    rows = despiked_window[HALO - 8 : HALO + frames]
    numer = sum_over_vox(precise_product(rows, tissue.T))
    voxel_signals = numer / float(tissue.shape[1] * lax.axis_size("vox"))

    first = lax.axis_index("tm") == 0
    base_before = jnp.concatenate([motion_before, voxel_signals[7:8]], axis=1)
    base_before = jnp.where(first, jnp.zeros_like(base_before), base_before)
    base_regressors = jnp.concatenate([motion, voxel_signals[8:]], axis=1)
    previous = jnp.concatenate([base_before, base_regressors[:-1]], axis=0)
    temporal_derivative = base_regressors - previous
    nuisance_matrix = jnp.concatenate(
        [
            base_regressors,
            temporal_derivative,
            base_regressors * base_regressors,
            temporal_derivative * temporal_derivative,
        ],
        axis=1,
    )
    terms = nuisance_matrix.shape[1]
    gram_matrix = precise_product(nuisance_matrix.T, nuisance_matrix)
    cross_products = precise_product(nuisance_matrix.T, spike_free_series)
    gram_rows = -(-terms * terms // voxels)
    gram_flat = jnp.pad(gram_matrix.reshape(terms * terms), (0, gram_rows * voxels - terms * terms))
    packed = jnp.concatenate([cross_products, gram_flat.reshape(gram_rows, voxels)], axis=0)
    summed = sum_over_tm(packed)
    cross_products = summed[:terms]
    gram_matrix = summed[terms:].reshape(-1)[: terms * terms].reshape(terms, terms)
    factor = jnp.linalg.cholesky(gram_matrix)
    weights = jax.scipy.linalg.cho_solve((factor, True), nuisance_matrix.T)
    return spike_free_series - precise_product(weights.T, cross_products)


def solution(mesh):
    return jax.shard_map(
        local,
        mesh=mesh,
        in_specs=(P("tm", "vox"), P("tm", "vox"), P("tm", None), P(None, "vox")),
        out_specs=P("tm", "vox"),
        check_vma=False,
    )
```

```python
import jax
import jax.numpy as jnp
from jax import lax
from jax.sharding import PartitionSpec as P

LEVELS = 4
HALO = 16


def from_behind(block, axis, distance):
    devices = range(lax.axis_size(axis))
    route = [((i - distance) % len(devices), i) for i in devices]
    return lax.ppermute(block, axis, route)


def precise_product(left, right):
    return jnp.dot(left, right, precision=lax.Precision.HIGHEST, preferred_element_type=jnp.float32)


def keep_level(spikes, level):
    return 1.0 - (spikes // 2**level % 2).astype(jnp.float32)


def despike_trimmed(window, flags):
    length = window.shape[0]
    approx = window
    start = 0
    kept_list = []
    for level in range(LEVELS):
        shift_rows = 2**level
        current, lagged = approx[shift_rows:], approx[:-shift_rows]
        start += shift_rows
        keep = keep_level(flags[start:], level)
        kept_list.append((start, (current - lagged) * 0.5 * keep))
        approx = (current + lagged) * 0.5
    for level in range(LEVELS - 1, -1, -1):
        shift_rows = 2**level
        kept_start, kept = kept_list[level]
        kept = kept[start - kept_start : start - kept_start + approx.shape[0]]
        approx = (approx[:-shift_rows] + approx[shift_rows:]) * 0.5 + (kept[:-shift_rows] - kept[shift_rows:]) * 0.5
    return approx


def sum_over_vox(block):
    n = lax.axis_size("vox")
    copies = jnp.broadcast_to(block, (n,) + block.shape)
    return lax.all_to_all(copies, "vox", 0, 0, tiled=False).sum(axis=0)


def sum_over_tm(block):
    n = lax.axis_size("tm")
    rows, cols = block.shape
    parts = block.reshape(rows, n, cols // n).transpose(1, 0, 2)
    owned = lax.all_to_all(parts, "tm", 0, 0, tiled=False).sum(axis=0)
    copies = jnp.broadcast_to(owned, (n,) + owned.shape)
    gathered = lax.all_to_all(copies, "tm", 0, 0, tiled=False)
    return gathered.transpose(1, 0, 2).reshape(rows, cols)


def local(series, spikes, motion, tissue):
    frames = series.shape[0]
    voxels = series.shape[1]
    motion_row = jnp.pad(motion[frames - 1 :], ((0, 7), (0, voxels - motion.shape[1])))
    tail = jnp.concatenate([series[frames - HALO :], spikes[frames - HALO :].astype(jnp.float32), motion_row], axis=0)
    head = jnp.concatenate([series[:HALO], spikes[:HALO].astype(jnp.float32)], axis=0)
    before = from_behind(tail, "tm", 1)
    after = from_behind(head, "tm", -1)
    motion_before = before[2 * HALO : 2 * HALO + 1, : motion.shape[1]]
    inner = despike_trimmed(series, spikes)
    edge = 2 * HALO
    head_window = despike_trimmed(
        jnp.concatenate([before[:HALO], series[:edge]], axis=0),
        jnp.concatenate([before[HALO : 2 * HALO].astype(jnp.int32), spikes[:edge]], axis=0),
    )
    tail_window = despike_trimmed(
        jnp.concatenate([series[frames - edge :], after[:HALO]], axis=0),
        jnp.concatenate([spikes[frames - edge :], after[HALO:].astype(jnp.int32)], axis=0),
    )
    middle = inner[1 : frames - 31]
    head_rows, tail_rows = head_window[: HALO + 1], tail_window[1 : HALO + 1]
    spike_free_series = jnp.concatenate([head_rows[1:], middle, tail_rows], axis=0)
    weights_t = tissue.T
    numer = jnp.concatenate(
        [
            jnp.zeros((7, tissue.shape[0]), jnp.float32),
            precise_product(head_rows, weights_t),
            precise_product(middle, weights_t),
            precise_product(tail_rows, weights_t),
        ],
        axis=0,
    )
    numer = sum_over_vox(numer)
    voxel_signals = numer / float(tissue.shape[1] * lax.axis_size("vox"))

    first = lax.axis_index("tm") == 0
    motion_before = jnp.where(first, jnp.zeros_like(motion_before), motion_before)
    motion_derivative = motion - jnp.concatenate([motion_before, motion[:-1]], axis=0)
    motion_terms = jnp.concatenate(
        [motion, motion_derivative, motion * motion, motion_derivative * motion_derivative], axis=1
    )
    inner_rows = slice(HALO, frames - HALO)
    motion_cross = (
        precise_product(motion_terms[inner_rows].T, middle)
        + precise_product(motion_terms[:HALO].T, head_rows[1:])
        + precise_product(motion_terms[frames - HALO :].T, tail_rows)
    )
    motion_gram = precise_product(motion_terms.T, motion_terms)

    signals_before = jnp.where(first, jnp.zeros_like(voxel_signals[7:8]), voxel_signals[7:8])
    signals = voxel_signals[8:]
    signal_derivative = signals - jnp.concatenate([signals_before, signals[:-1]], axis=0)
    signal_terms = jnp.concatenate(
        [signals, signal_derivative, signals * signals, signal_derivative * signal_derivative], axis=1
    )
    nuisance_matrix = jnp.concatenate([motion_terms, signal_terms], axis=1)
    signal_cross = precise_product(signal_terms.T, spike_free_series)
    signal_gram = precise_product(signal_terms.T, nuisance_matrix)
    moving, signaled = motion_terms.shape[1], signal_terms.shape[1]
    terms = moving + signaled
    gram_matrix = jnp.concatenate(
        [jnp.concatenate([motion_gram, signal_gram[:, :moving].T], axis=1), signal_gram], axis=0
    )
    cross_products = jnp.concatenate([motion_cross, signal_cross], axis=0)
    gram_rows = -(-terms * terms // voxels)
    gram_flat = jnp.pad(gram_matrix.reshape(terms * terms), (0, gram_rows * voxels - terms * terms))
    packed = jnp.concatenate([cross_products, gram_flat.reshape(gram_rows, voxels)], axis=0)
    summed = sum_over_tm(packed)
    cross_products = summed[:terms]
    gram_matrix = summed[terms:].reshape(-1)[: terms * terms].reshape(terms, terms)
    factor = jnp.linalg.cholesky(gram_matrix)
    weights = jax.scipy.linalg.cho_solve((factor, True), nuisance_matrix.T)
    return spike_free_series - precise_product(weights.T, cross_products)


def solution(mesh):
    return jax.shard_map(
        local,
        mesh=mesh,
        in_specs=(P("tm", "vox"), P("tm", "vox"), P("tm", None), P(None, "vox")),
        out_specs=P("tm", "vox"),
        check_vma=False,
    )
```

```python
import jax
import jax.numpy as jnp
from jax import lax
from jax.sharding import PartitionSpec as P

LEVELS = 4
HALO = 16


def from_behind(block, axis, distance):
    devices = range(lax.axis_size(axis))
    route = [((i - distance) % len(devices), i) for i in devices]
    return lax.ppermute(block, axis, route)


def precise_product(left, right):
    return jnp.dot(left, right, precision=lax.Precision.HIGHEST, preferred_element_type=jnp.float32)


def keep_level(spikes, level):
    return 1.0 - (spikes // 2**level % 2).astype(jnp.float32)


def despike_trimmed(window, flags):
    length = window.shape[0]
    approx = window
    start = 0
    kept_list = []
    for level in range(LEVELS):
        shift_rows = 2**level
        current, lagged = approx[shift_rows:], approx[:-shift_rows]
        start += shift_rows
        keep = keep_level(flags[start:], level)
        kept_list.append((start, (current - lagged) * 0.5 * keep))
        approx = (current + lagged) * 0.5
    for level in range(LEVELS - 1, -1, -1):
        shift_rows = 2**level
        kept_start, kept = kept_list[level]
        kept = kept[start - kept_start : start - kept_start + approx.shape[0]]
        approx = (approx[:-shift_rows] + approx[shift_rows:]) * 0.5 + (kept[:-shift_rows] - kept[shift_rows:]) * 0.5
    return approx


def sum_over_vox(block):
    n = lax.axis_size("vox")
    flat = block.reshape(1, block.size)
    copies = jnp.broadcast_to(flat, (n,) + flat.shape)
    return lax.all_to_all(copies, "vox", 0, 0, tiled=False).sum(axis=0).reshape(block.shape)


def sum_over_tm(block):
    n = lax.axis_size("tm")
    rows, cols = block.shape
    parts = block.reshape(rows, n, cols // n).transpose(1, 0, 2)
    owned = lax.all_to_all(parts, "tm", 0, 0, tiled=False).sum(axis=0)
    copies = jnp.broadcast_to(owned, (n,) + owned.shape)
    gathered = lax.all_to_all(copies, "tm", 0, 0, tiled=False)
    return gathered.transpose(1, 0, 2).reshape(rows, cols)


def local(series, spikes, motion, tissue):
    frames = series.shape[0]
    voxels = series.shape[1]
    motion_row = jnp.pad(motion[frames - 1 :], ((0, 7), (0, voxels - motion.shape[1])))
    tail = jnp.concatenate([series[frames - HALO :], spikes[frames - HALO :].astype(jnp.float32), motion_row], axis=0)
    head = jnp.concatenate([series[:HALO], spikes[:HALO].astype(jnp.float32)], axis=0)
    before = from_behind(tail, "tm", 1)
    after = from_behind(head, "tm", -1)
    motion_before = before[2 * HALO : 2 * HALO + 1, : motion.shape[1]]
    inner = despike_trimmed(series, spikes)
    edge = 2 * HALO
    head_window = despike_trimmed(
        jnp.concatenate([before[:HALO], series[:edge]], axis=0),
        jnp.concatenate([before[HALO : 2 * HALO].astype(jnp.int32), spikes[:edge]], axis=0),
    )
    tail_window = despike_trimmed(
        jnp.concatenate([series[frames - edge :], after[:HALO]], axis=0),
        jnp.concatenate([spikes[frames - edge :], after[HALO:].astype(jnp.int32)], axis=0),
    )
    spike_free_series = jnp.concatenate([head_window[1 : HALO + 1], inner[1 : frames - 31], tail_window[1 : HALO + 1]], axis=0)
    despiked_window = jnp.concatenate([jnp.zeros((HALO - 1, voxels), jnp.float32), head_window[:1], spike_free_series], axis=0)

    rows = despiked_window[HALO - 8 : HALO + frames]
    numer = sum_over_vox(precise_product(rows, tissue.T))
    voxel_signals = numer / float(tissue.shape[1] * lax.axis_size("vox"))

    first = lax.axis_index("tm") == 0
    base_before = jnp.concatenate([motion_before, voxel_signals[7:8]], axis=1)
    base_before = jnp.where(first, jnp.zeros_like(base_before), base_before)
    base_regressors = jnp.concatenate([motion, voxel_signals[8:]], axis=1)
    previous = jnp.concatenate([base_before, base_regressors[:-1]], axis=0)
    temporal_derivative = base_regressors - previous
    nuisance_matrix = jnp.concatenate(
        [
            base_regressors,
            temporal_derivative,
            base_regressors * base_regressors,
            temporal_derivative * temporal_derivative,
        ],
        axis=1,
    )
    terms = nuisance_matrix.shape[1]
    gram_matrix = precise_product(nuisance_matrix.T, nuisance_matrix)
    cross_products = precise_product(nuisance_matrix.T, spike_free_series)
    gram_rows = -(-terms * terms // voxels)
    gram_flat = jnp.pad(gram_matrix.reshape(terms * terms), (0, gram_rows * voxels - terms * terms))
    packed = jnp.concatenate([cross_products, gram_flat.reshape(gram_rows, voxels)], axis=0)
    summed = sum_over_tm(packed)
    cross_products = summed[:terms]
    gram_matrix = summed[terms:].reshape(-1)[: terms * terms].reshape(terms, terms)
    factor = jnp.linalg.cholesky(gram_matrix)
    weights = jax.scipy.linalg.cho_solve((factor, True), nuisance_matrix.T)
    return spike_free_series - precise_product(weights.T, cross_products)


def solution(mesh):
    return jax.shard_map(
        local,
        mesh=mesh,
        in_specs=(P("tm", "vox"), P("tm", "vox"), P("tm", None), P(None, "vox")),
        out_specs=P("tm", "vox"),
        check_vma=False,
    )
```

```python
import jax
import jax.numpy as jnp
from jax import lax
from jax.sharding import PartitionSpec as P

LEVELS = 4
HALO = 16


def from_behind(block, axis, distance):
    devices = range(lax.axis_size(axis))
    route = [((i - distance) % len(devices), i) for i in devices]
    return lax.ppermute(block, axis, route)


def precise_product(left, right):
    return jnp.dot(left, right, precision=lax.Precision.HIGHEST, preferred_element_type=jnp.float32)


def keep_level(spikes, level):
    return 1.0 - (spikes // 2**level % 2).astype(jnp.float32)


def despike_trimmed(window, flags):
    length = window.shape[0]
    approx = window
    start = 0
    kept_list = []
    for level in range(LEVELS):
        shift_rows = 2**level
        current, lagged = approx[shift_rows:], approx[:-shift_rows]
        start += shift_rows
        keep = keep_level(flags[start:], level)
        kept_list.append((start, (current - lagged) * 0.5 * keep))
        approx = (current + lagged) * 0.5
    for level in range(LEVELS - 1, -1, -1):
        shift_rows = 2**level
        kept_start, kept = kept_list[level]
        kept = kept[start - kept_start : start - kept_start + approx.shape[0]]
        approx = (approx[:-shift_rows] + approx[shift_rows:]) * 0.5 + (kept[:-shift_rows] - kept[shift_rows:]) * 0.5
    return approx


def sum_over_vox(block):
    n = lax.axis_size("vox")
    flat = block.reshape(1, block.size)
    copies = jnp.broadcast_to(flat, (n,) + flat.shape)
    return lax.all_to_all(copies, "vox", 0, 0, tiled=False).sum(axis=0).reshape(block.shape)


def sum_over_tm(block):
    n = lax.axis_size("tm")
    rows, cols = block.shape
    parts = block.reshape(rows, n, cols // n).transpose(1, 0, 2)
    owned = lax.all_to_all(parts, "tm", 0, 0, tiled=False).sum(axis=0)
    copies = jnp.broadcast_to(owned, (n,) + owned.shape)
    gathered = lax.all_to_all(copies, "tm", 0, 0, tiled=False)
    return gathered.transpose(1, 0, 2).reshape(rows, cols)


def local(series, spikes, motion, tissue):
    frames = series.shape[0]
    voxels = series.shape[1]
    motion_row = jnp.pad(motion[frames - 1 :], ((0, 7), (0, voxels - motion.shape[1])))
    tail = jnp.concatenate([series[frames - HALO :], spikes[frames - HALO :].astype(jnp.float32), motion_row], axis=0)
    head = jnp.concatenate([series[:HALO], spikes[:HALO].astype(jnp.float32)], axis=0)
    before = from_behind(tail, "tm", 1)
    after = from_behind(head, "tm", -1)
    motion_before = before[2 * HALO : 2 * HALO + 1, : motion.shape[1]]
    inner = despike_trimmed(series, spikes)
    edge = 2 * HALO
    head_window = despike_trimmed(
        jnp.concatenate([before[:HALO], series[:edge]], axis=0),
        jnp.concatenate([before[HALO : 2 * HALO].astype(jnp.int32), spikes[:edge]], axis=0),
    )
    tail_window = despike_trimmed(
        jnp.concatenate([series[frames - edge :], after[:HALO]], axis=0),
        jnp.concatenate([spikes[frames - edge :], after[HALO:].astype(jnp.int32)], axis=0),
    )
    spike_free_series = jnp.concatenate([head_window[1 : HALO + 1], inner[1 : frames - 31], tail_window[1 : HALO + 1]], axis=0)
    despiked_window = jnp.concatenate([jnp.zeros((HALO - 1, voxels), jnp.float32), head_window[:1], spike_free_series], axis=0)

    rows = despiked_window[HALO - 8 : HALO + frames]
    numer = sum_over_vox(precise_product(rows, tissue.T))
    voxel_signals = numer / float(tissue.shape[1] * lax.axis_size("vox"))

    first = lax.axis_index("tm") == 0
    base_before = jnp.concatenate([motion_before, voxel_signals[7:8]], axis=1)
    base_before = jnp.where(first, jnp.zeros_like(base_before), base_before)
    base_regressors = jnp.concatenate([motion, voxel_signals[8:]], axis=1)
    previous = jnp.concatenate([base_before, base_regressors[:-1]], axis=0)
    temporal_derivative = base_regressors - previous
    nuisance_matrix = jnp.concatenate(
        [
            base_regressors,
            temporal_derivative,
            base_regressors * base_regressors,
            temporal_derivative * temporal_derivative,
        ],
        axis=1,
    )
    terms = nuisance_matrix.shape[1]
    gram_matrix = precise_product(nuisance_matrix.T, nuisance_matrix)
    cross_products = precise_product(nuisance_matrix.T, spike_free_series)
    gram_rows = -(-terms * terms // voxels)
    gram_flat = jnp.pad(gram_matrix.reshape(terms * terms), (0, gram_rows * voxels - terms * terms))
    packed = jnp.concatenate([cross_products, gram_flat.reshape(gram_rows, voxels)], axis=0)
    summed = sum_over_tm(packed)
    cross_products = summed[:terms]
    gram_matrix = summed[terms:].reshape(-1)[: terms * terms].reshape(terms, terms)
    factor = jnp.linalg.cholesky(gram_matrix)
    weights = jax.scipy.linalg.cho_solve((factor, True), nuisance_matrix.T)
    fit = jnp.dot(weights.T, cross_products, precision=lax.Precision.HIGH, preferred_element_type=jnp.float32)
    return spike_free_series - fit


def solution(mesh):
    return jax.shard_map(
        local,
        mesh=mesh,
        in_specs=(P("tm", "vox"), P("tm", "vox"), P("tm", None), P(None, "vox")),
        out_specs=P("tm", "vox"),
        check_vma=False,
    )
```

```python
import jax
import jax.numpy as jnp
from jax import lax
from jax.sharding import PartitionSpec as P
from jax.experimental import pallas as pl

LEVELS = 4
HALO = 16


def from_behind(block, axis, distance):
    devices = range(lax.axis_size(axis))
    route = [((i - distance) % len(devices), i) for i in devices]
    return lax.ppermute(block, axis, route)


def precise_product(left, right):
    return jnp.dot(left, right, precision=lax.Precision.HIGHEST, preferred_element_type=jnp.float32)


def keep_level(spikes, level):
    return 1.0 - (spikes // 2**level % 2).astype(jnp.float32)


def despike_trimmed(window, flags):
    length = window.shape[0]
    approx = window
    start = 0
    kept_list = []
    for level in range(LEVELS):
        shift_rows = 2**level
        current, lagged = approx[shift_rows:], approx[:-shift_rows]
        start += shift_rows
        keep = keep_level(flags[start:], level)
        kept_list.append((start, (current - lagged) * 0.5 * keep))
        approx = (current + lagged) * 0.5
    for level in range(LEVELS - 1, -1, -1):
        shift_rows = 2**level
        kept_start, kept = kept_list[level]
        kept = kept[start - kept_start : start - kept_start + approx.shape[0]]
        approx = (approx[:-shift_rows] + approx[shift_rows:]) * 0.5 + (kept[:-shift_rows] - kept[shift_rows:]) * 0.5
    return approx


def sum_over_vox(block):
    n = lax.axis_size("vox")
    flat = block.reshape(1, block.size)
    copies = jnp.broadcast_to(flat, (n,) + flat.shape)
    return lax.all_to_all(copies, "vox", 0, 0, tiled=False).sum(axis=0).reshape(block.shape)


def sum_over_tm(block):
    n = lax.axis_size("tm")
    rows, cols = block.shape
    parts = block.reshape(rows, n, cols // n).transpose(1, 0, 2)
    owned = lax.all_to_all(parts, "tm", 0, 0, tiled=False).sum(axis=0)
    copies = jnp.broadcast_to(owned, (n,) + owned.shape)
    gathered = lax.all_to_all(copies, "tm", 0, 0, tiled=False)
    return gathered.transpose(1, 0, 2).reshape(rows, cols)


def solve_kernel(terms, gram_ref, rhs_ref, out_ref):
    size = gram_ref.shape[0]
    sub = lax.broadcasted_iota(jnp.int32, (size, size), 0)
    lane = lax.broadcasted_iota(jnp.int32, (size, size), 1)
    rsub = lax.broadcasted_iota(jnp.int32, rhs_ref.shape, 0)

    def factor_step(k, carry):
        a, low, low_t = carry
        col = jnp.sum(jnp.where(lane == k, a, 0.0), axis=1, keepdims=True)
        row = jnp.sum(jnp.where(sub == k, a, 0.0), axis=0, keepdims=True)
        root = jnp.sqrt(jnp.sum(jnp.where(lane[:1] == k, row, 0.0)))
        lcol = jnp.where(sub[:, :1] >= k, col / root, 0.0)
        lrow = jnp.where(lane[:1] >= k, row / root, 0.0)
        return a - lcol * lrow, low + jnp.where(lane == k, lcol, 0.0), low_t + jnp.where(sub == k, lrow, 0.0)

    zero = jnp.zeros((size, size), jnp.float32)
    _, low, low_t = lax.fori_loop(0, terms, factor_step, (gram_ref[...], zero, zero))
    diag = jnp.sum(jnp.where(sub == lane, low, 0.0), axis=1, keepdims=True)

    def forward(k, carry):
        b, y = carry
        yk = jnp.sum(jnp.where(rsub == k, b, 0.0), axis=0, keepdims=True) / jnp.sum(jnp.where(sub[:, :1] == k, diag, 0.0))
        lcol = jnp.sum(jnp.where(lane == k, low, 0.0), axis=1, keepdims=True)
        return b - lcol * yk, y + jnp.where(rsub == k, yk, 0.0)

    _, y = lax.fori_loop(0, terms, forward, (rhs_ref[...], jnp.zeros(rhs_ref.shape, jnp.float32)))

    def backward(step, carry):
        k = terms - 1 - step
        y, x = carry
        xk = jnp.sum(jnp.where(rsub == k, y, 0.0), axis=0, keepdims=True) / jnp.sum(jnp.where(sub[:, :1] == k, diag, 0.0))
        ucol = jnp.where(sub[:, :1] < k, jnp.sum(jnp.where(lane == k, low_t, 0.0), axis=1, keepdims=True), 0.0)
        return y - ucol * xk, x + jnp.where(rsub == k, xk, 0.0)

    _, x = lax.fori_loop(0, terms, backward, (y, jnp.zeros(rhs_ref.shape, jnp.float32)))
    out_ref[...] = x


def cholesky_solve(gram_matrix, rhs):
    terms = gram_matrix.shape[0]
    size = 128
    padded = jnp.eye(size, dtype=jnp.float32).at[:terms, :terms].set(gram_matrix)
    rows = -(-terms // 8) * 8
    rhs_padded = jnp.pad(rhs, ((0, size - terms), (0, 0)))
    out = pl.pallas_call(
        lambda g, b, o: solve_kernel(terms, g, b, o),
        out_shape=jax.ShapeDtypeStruct(rhs_padded.shape, jnp.float32),
    )(padded, rhs_padded)
    return out[:terms]


def local(series, spikes, motion, tissue):
    frames = series.shape[0]
    voxels = series.shape[1]
    motion_row = jnp.pad(motion[frames - 1 :], ((0, 7), (0, voxels - motion.shape[1])))
    tail = jnp.concatenate([series[frames - HALO :], spikes[frames - HALO :].astype(jnp.float32), motion_row], axis=0)
    head = jnp.concatenate([series[:HALO], spikes[:HALO].astype(jnp.float32)], axis=0)
    before = from_behind(tail, "tm", 1)
    after = from_behind(head, "tm", -1)
    motion_before = before[2 * HALO : 2 * HALO + 1, : motion.shape[1]]
    inner = despike_trimmed(series, spikes)
    edge = 2 * HALO
    head_window = despike_trimmed(
        jnp.concatenate([before[:HALO], series[:edge]], axis=0),
        jnp.concatenate([before[HALO : 2 * HALO].astype(jnp.int32), spikes[:edge]], axis=0),
    )
    tail_window = despike_trimmed(
        jnp.concatenate([series[frames - edge :], after[:HALO]], axis=0),
        jnp.concatenate([spikes[frames - edge :], after[HALO:].astype(jnp.int32)], axis=0),
    )
    spike_free_series = jnp.concatenate([head_window[1 : HALO + 1], inner[1 : frames - 31], tail_window[1 : HALO + 1]], axis=0)
    despiked_window = jnp.concatenate([jnp.zeros((HALO - 1, voxels), jnp.float32), head_window[:1], spike_free_series], axis=0)

    rows = despiked_window[HALO - 8 : HALO + frames]
    numer = sum_over_vox(precise_product(rows, tissue.T))
    voxel_signals = numer / float(tissue.shape[1] * lax.axis_size("vox"))

    first = lax.axis_index("tm") == 0
    base_before = jnp.concatenate([motion_before, voxel_signals[7:8]], axis=1)
    base_before = jnp.where(first, jnp.zeros_like(base_before), base_before)
    base_regressors = jnp.concatenate([motion, voxel_signals[8:]], axis=1)
    previous = jnp.concatenate([base_before, base_regressors[:-1]], axis=0)
    temporal_derivative = base_regressors - previous
    nuisance_matrix = jnp.concatenate(
        [
            base_regressors,
            temporal_derivative,
            base_regressors * base_regressors,
            temporal_derivative * temporal_derivative,
        ],
        axis=1,
    )
    terms = nuisance_matrix.shape[1]
    gram_matrix = precise_product(nuisance_matrix.T, nuisance_matrix)
    cross_products = precise_product(nuisance_matrix.T, spike_free_series)
    gram_rows = -(-terms * terms // voxels)
    gram_flat = jnp.pad(gram_matrix.reshape(terms * terms), (0, gram_rows * voxels - terms * terms))
    packed = jnp.concatenate([cross_products, gram_flat.reshape(gram_rows, voxels)], axis=0)
    summed = sum_over_tm(packed)
    cross_products = summed[:terms]
    gram_matrix = summed[terms:].reshape(-1)[: terms * terms].reshape(terms, terms)
    weights = cholesky_solve(gram_matrix, nuisance_matrix.T)
    return spike_free_series - precise_product(weights.T, cross_products)


def solution(mesh):
    return jax.shard_map(
        local,
        mesh=mesh,
        in_specs=(P("tm", "vox"), P("tm", "vox"), P("tm", None), P(None, "vox")),
        out_specs=P("tm", "vox"),
        check_vma=False,
    )
```

```python
import jax
import jax.numpy as jnp
from jax import lax
from jax.sharding import PartitionSpec as P

LEVELS = 4
HALO = 16


def from_behind(block, axis, distance):
    devices = range(lax.axis_size(axis))
    route = [((i - distance) % len(devices), i) for i in devices]
    return lax.ppermute(block, axis, route)


def precise_product(left, right):
    return jnp.dot(left, right, precision=lax.Precision.HIGHEST, preferred_element_type=jnp.float32)


def keep_level(spikes, level):
    return 1.0 - (spikes // 2**level % 2).astype(jnp.float32)


def despike_trimmed(window, flags):
    length = window.shape[0]
    approx = window
    start = 0
    kept_list = []
    for level in range(LEVELS):
        shift_rows = 2**level
        current, lagged = approx[shift_rows:], approx[:-shift_rows]
        start += shift_rows
        keep = keep_level(flags[start:], level)
        kept_list.append((start, (current - lagged) * 0.5 * keep))
        approx = (current + lagged) * 0.5
    for level in range(LEVELS - 1, -1, -1):
        shift_rows = 2**level
        kept_start, kept = kept_list[level]
        kept = kept[start - kept_start : start - kept_start + approx.shape[0]]
        approx = (approx[:-shift_rows] + approx[shift_rows:]) * 0.5 + (kept[:-shift_rows] - kept[shift_rows:]) * 0.5
    return approx


def sum_over_vox(block):
    n = lax.axis_size("vox")
    pair = block + lax.ppermute(block, "vox", [(i, i ^ 1) for i in range(n)])
    flat = pair.reshape(1, pair.size)
    copies = jnp.broadcast_to(flat, (n // 2,) + flat.shape)
    groups = [list(range(0, n, 2)), list(range(1, n, 2))]
    got = lax.all_to_all(copies, "vox", 0, 0, axis_index_groups=groups, tiled=False)
    return got.sum(axis=0).reshape(block.shape)


def sum_over_tm(block):
    n = lax.axis_size("tm")
    rows, cols = block.shape
    parts = block.reshape(rows, n, cols // n).transpose(1, 0, 2)
    owned = lax.all_to_all(parts, "tm", 0, 0, tiled=False).sum(axis=0)
    copies = jnp.broadcast_to(owned, (n,) + owned.shape)
    gathered = lax.all_to_all(copies, "tm", 0, 0, tiled=False)
    return gathered.transpose(1, 0, 2).reshape(rows, cols)


def local(series, spikes, motion, tissue):
    frames = series.shape[0]
    voxels = series.shape[1]
    motion_row = jnp.pad(motion[frames - 1 :], ((0, 7), (0, voxels - motion.shape[1])))
    tail = jnp.concatenate([series[frames - HALO :], spikes[frames - HALO :].astype(jnp.float32), motion_row], axis=0)
    head = jnp.concatenate([series[:HALO], spikes[:HALO].astype(jnp.float32)], axis=0)
    before = from_behind(tail, "tm", 1)
    after = from_behind(head, "tm", -1)
    motion_before = before[2 * HALO : 2 * HALO + 1, : motion.shape[1]]
    inner = despike_trimmed(series, spikes)
    edge = 2 * HALO
    head_window = despike_trimmed(
        jnp.concatenate([before[:HALO], series[:edge]], axis=0),
        jnp.concatenate([before[HALO : 2 * HALO].astype(jnp.int32), spikes[:edge]], axis=0),
    )
    tail_window = despike_trimmed(
        jnp.concatenate([series[frames - edge :], after[:HALO]], axis=0),
        jnp.concatenate([spikes[frames - edge :], after[HALO:].astype(jnp.int32)], axis=0),
    )
    spike_free_series = jnp.concatenate([head_window[1 : HALO + 1], inner[1 : frames - 31], tail_window[1 : HALO + 1]], axis=0)
    despiked_window = jnp.concatenate([jnp.zeros((HALO - 1, voxels), jnp.float32), head_window[:1], spike_free_series], axis=0)

    rows = despiked_window[HALO - 8 : HALO + frames]
    numer = sum_over_vox(precise_product(rows, tissue.T))
    voxel_signals = numer / float(tissue.shape[1] * lax.axis_size("vox"))

    first = lax.axis_index("tm") == 0
    base_before = jnp.concatenate([motion_before, voxel_signals[7:8]], axis=1)
    base_before = jnp.where(first, jnp.zeros_like(base_before), base_before)
    base_regressors = jnp.concatenate([motion, voxel_signals[8:]], axis=1)
    previous = jnp.concatenate([base_before, base_regressors[:-1]], axis=0)
    temporal_derivative = base_regressors - previous
    nuisance_matrix = jnp.concatenate(
        [
            base_regressors,
            temporal_derivative,
            base_regressors * base_regressors,
            temporal_derivative * temporal_derivative,
        ],
        axis=1,
    )
    terms = nuisance_matrix.shape[1]
    gram_matrix = precise_product(nuisance_matrix.T, nuisance_matrix)
    cross_products = precise_product(nuisance_matrix.T, spike_free_series)
    gram_rows = -(-terms * terms // voxels)
    gram_flat = jnp.pad(gram_matrix.reshape(terms * terms), (0, gram_rows * voxels - terms * terms))
    packed = jnp.concatenate([cross_products, gram_flat.reshape(gram_rows, voxels)], axis=0)
    summed = sum_over_tm(packed)
    cross_products = summed[:terms]
    gram_matrix = summed[terms:].reshape(-1)[: terms * terms].reshape(terms, terms)
    factor = jnp.linalg.cholesky(gram_matrix)
    weights = jax.scipy.linalg.cho_solve((factor, True), nuisance_matrix.T)
    return spike_free_series - precise_product(weights.T, cross_products)


def solution(mesh):
    return jax.shard_map(
        local,
        mesh=mesh,
        in_specs=(P("tm", "vox"), P("tm", "vox"), P("tm", None), P(None, "vox")),
        out_specs=P("tm", "vox"),
        check_vma=False,
    )
```

```python
import jax
import jax.numpy as jnp
from jax import lax
from jax.sharding import PartitionSpec as P

LEVELS = 4
HALO = 16


def from_behind(block, axis, distance):
    devices = range(lax.axis_size(axis))
    route = [((i - distance) % len(devices), i) for i in devices]
    return lax.ppermute(block, axis, route)


def precise_product(left, right):
    return jnp.dot(left, right, precision=lax.Precision.HIGHEST, preferred_element_type=jnp.float32)


def keep_level(spikes, level):
    return 1.0 - (spikes // 2**level % 2).astype(jnp.float32)


def despike_trimmed(window, flags):
    length = window.shape[0]
    approx = window
    start = 0
    kept_list = []
    for level in range(LEVELS):
        shift_rows = 2**level
        current, lagged = approx[shift_rows:], approx[:-shift_rows]
        start += shift_rows
        keep = keep_level(flags[start:], level)
        kept_list.append((start, (current - lagged) * 0.5 * keep))
        approx = (current + lagged) * 0.5
    for level in range(LEVELS - 1, -1, -1):
        shift_rows = 2**level
        kept_start, kept = kept_list[level]
        kept = kept[start - kept_start : start - kept_start + approx.shape[0]]
        approx = (approx[:-shift_rows] + approx[shift_rows:]) * 0.5 + (kept[:-shift_rows] - kept[shift_rows:]) * 0.5
    return approx


def sum_over_vox(block):
    n = lax.axis_size("vox")
    flat = block.reshape(1, block.size)
    copies = jnp.broadcast_to(flat, (n,) + flat.shape)
    return lax.all_to_all(copies, "vox", 0, 0, tiled=False).sum(axis=0).reshape(block.shape)


def sum_over_tm(block):
    n = lax.axis_size("tm")
    rows, cols = block.shape
    parts = block.reshape(rows, n, cols // n).transpose(1, 0, 2)
    owned = lax.all_to_all(parts, "tm", 0, 0, tiled=False).sum(axis=0)
    copies = jnp.broadcast_to(owned, (n,) + owned.shape)
    gathered = lax.all_to_all(copies, "tm", 0, 0, tiled=False)
    return gathered.transpose(1, 0, 2).reshape(rows, cols)


def local(series, spikes, motion, tissue):
    frames = series.shape[0]
    voxels = series.shape[1]
    motion_row = jnp.pad(motion[frames - 1 :], ((0, 7), (0, voxels - motion.shape[1])))
    tail = jnp.concatenate([series[frames - HALO :], spikes[frames - HALO :].astype(jnp.float32), motion_row], axis=0)
    head = jnp.concatenate([series[:HALO], spikes[:HALO].astype(jnp.float32)], axis=0)
    before = from_behind(tail, "tm", 1)
    after = from_behind(head, "tm", -1)
    motion_before = before[2 * HALO : 2 * HALO + 1, : motion.shape[1]]
    inner = despike_trimmed(series, spikes)
    edge = 2 * HALO
    head_window = despike_trimmed(
        jnp.concatenate([before[:HALO], series[:edge]], axis=0),
        jnp.concatenate([before[HALO : 2 * HALO].astype(jnp.int32), spikes[:edge]], axis=0),
    )
    tail_window = despike_trimmed(
        jnp.concatenate([series[frames - edge :], after[:HALO]], axis=0),
        jnp.concatenate([spikes[frames - edge :], after[HALO:].astype(jnp.int32)], axis=0),
    )
    spike_free_series = jnp.concatenate([head_window[1 : HALO + 1], inner[1 : frames - 31], tail_window[1 : HALO + 1]], axis=0)

    rows = jnp.concatenate([head_window[:1], spike_free_series], axis=0)
    numer = sum_over_vox(precise_product(rows, tissue.T))
    voxel_signals = jnp.pad(numer, ((7, 0), (0, 0))) / float(tissue.shape[1] * lax.axis_size("vox"))

    first = lax.axis_index("tm") == 0
    base_before = jnp.concatenate([motion_before, voxel_signals[7:8]], axis=1)
    base_before = jnp.where(first, jnp.zeros_like(base_before), base_before)
    base_regressors = jnp.concatenate([motion, voxel_signals[8:]], axis=1)
    previous = jnp.concatenate([base_before, base_regressors[:-1]], axis=0)
    temporal_derivative = base_regressors - previous
    nuisance_matrix = jnp.concatenate(
        [
            base_regressors,
            temporal_derivative,
            base_regressors * base_regressors,
            temporal_derivative * temporal_derivative,
        ],
        axis=1,
    )
    terms = nuisance_matrix.shape[1]
    gram_matrix = precise_product(nuisance_matrix.T, nuisance_matrix)
    cross_products = precise_product(nuisance_matrix.T, spike_free_series)
    gram_rows = -(-terms * terms // voxels)
    gram_flat = jnp.pad(gram_matrix.reshape(terms * terms), (0, gram_rows * voxels - terms * terms))
    packed = jnp.concatenate([cross_products, gram_flat.reshape(gram_rows, voxels)], axis=0)
    summed = sum_over_tm(packed)
    cross_products = summed[:terms]
    gram_matrix = summed[terms:].reshape(-1)[: terms * terms].reshape(terms, terms)
    factor = jnp.linalg.cholesky(gram_matrix)
    weights = jax.scipy.linalg.cho_solve((factor, True), nuisance_matrix.T)
    return spike_free_series - precise_product(weights.T, cross_products)


def solution(mesh):
    return jax.shard_map(
        local,
        mesh=mesh,
        in_specs=(P("tm", "vox"), P("tm", "vox"), P("tm", None), P(None, "vox")),
        out_specs=P("tm", "vox"),
        check_vma=False,
    )
```

```python
import jax
import jax.numpy as jnp
from jax import lax
from jax.sharding import PartitionSpec as P

LEVELS = 4
HALO = 16


def from_behind(block, axis, distance):
    devices = range(lax.axis_size(axis))
    route = [((i - distance) % len(devices), i) for i in devices]
    return lax.ppermute(block, axis, route)


def precise_product(left, right):
    return jnp.dot(left, right, precision=lax.Precision.HIGHEST, preferred_element_type=jnp.float32)


def keep_level(spikes, level):
    return 1.0 - (spikes // 2**level % 2).astype(jnp.float32)


def despike_trimmed(window, flags):
    length = window.shape[0]
    approx = window
    start = 0
    kept_list = []
    for level in range(LEVELS):
        shift_rows = 2**level
        current, lagged = approx[shift_rows:], approx[:-shift_rows]
        start += shift_rows
        keep = keep_level(flags[start:], level)
        kept_list.append((start, (current - lagged) * 0.5 * keep))
        approx = (current + lagged) * 0.5
    for level in range(LEVELS - 1, -1, -1):
        shift_rows = 2**level
        kept_start, kept = kept_list[level]
        kept = kept[start - kept_start : start - kept_start + approx.shape[0]]
        approx = (approx[:-shift_rows] + approx[shift_rows:]) * 0.5 + (kept[:-shift_rows] - kept[shift_rows:]) * 0.5
    return approx


def sum_over_vox(block):
    n = lax.axis_size("vox")
    flat = block.reshape(1, block.size)
    copies = jnp.broadcast_to(flat, (n,) + flat.shape)
    return lax.all_to_all(copies, "vox", 0, 0, tiled=False).sum(axis=0).reshape(block.shape)


def sum_over_tm(block):
    n = lax.axis_size("tm")
    rows, cols = block.shape
    parts = block.reshape(rows, n, cols // n).transpose(1, 0, 2)
    owned = lax.all_to_all(parts, "tm", 0, 0, tiled=False).sum(axis=0)
    copies = jnp.broadcast_to(owned, (n,) + owned.shape)
    gathered = lax.all_to_all(copies, "tm", 0, 0, tiled=False)
    return gathered.transpose(1, 0, 2).reshape(rows, cols)


def local(series, spikes, motion, tissue):
    frames = series.shape[0]
    voxels = series.shape[1]
    last_rows = jnp.concatenate(
        [spikes[frames - 1 :].astype(jnp.float32), jnp.pad(motion[frames - 1 :], ((0, 0), (0, voxels - motion.shape[1])))],
        axis=0,
    )
    tail = jnp.concatenate([series[frames - HALO :], jnp.pad(last_rows, ((0, 6), (0, 0)))], axis=0)
    head = jnp.concatenate([series[:HALO], spikes[:HALO].astype(jnp.float32)], axis=0)
    after = from_behind(head, "tm", -1)
    before = from_behind(tail, "tm", 1)
    motion_before = before[HALO + 1 : HALO + 2, : motion.shape[1]]
    flags_before = jnp.concatenate(
        [jnp.zeros((HALO - 1, voxels), jnp.int32), before[HALO : HALO + 1].astype(jnp.int32)], axis=0
    )
    inner = despike_trimmed(series, spikes)
    edge = 2 * HALO
    head_window = despike_trimmed(
        jnp.concatenate([before[:HALO], series[:edge]], axis=0),
        jnp.concatenate([flags_before, spikes[:edge]], axis=0),
    )
    tail_window = despike_trimmed(
        jnp.concatenate([series[frames - edge :], after[:HALO]], axis=0),
        jnp.concatenate([spikes[frames - edge :], after[HALO:].astype(jnp.int32)], axis=0),
    )
    spike_free_series = jnp.concatenate([head_window[1 : HALO + 1], inner[1 : frames - 31], tail_window[1 : HALO + 1]], axis=0)

    rows = jnp.concatenate([head_window[:1], spike_free_series], axis=0)
    numer = sum_over_vox(precise_product(rows, tissue.T))
    voxel_signals = jnp.pad(numer, ((7, 0), (0, 0))) / float(tissue.shape[1] * lax.axis_size("vox"))

    first = lax.axis_index("tm") == 0
    base_before = jnp.concatenate([motion_before, voxel_signals[7:8]], axis=1)
    base_before = jnp.where(first, jnp.zeros_like(base_before), base_before)
    base_regressors = jnp.concatenate([motion, voxel_signals[8:]], axis=1)
    previous = jnp.concatenate([base_before, base_regressors[:-1]], axis=0)
    temporal_derivative = base_regressors - previous
    nuisance_matrix = jnp.concatenate(
        [
            base_regressors,
            temporal_derivative,
            base_regressors * base_regressors,
            temporal_derivative * temporal_derivative,
        ],
        axis=1,
    )
    terms = nuisance_matrix.shape[1]
    gram_matrix = precise_product(nuisance_matrix.T, nuisance_matrix)
    cross_products = precise_product(nuisance_matrix.T, spike_free_series)
    gram_rows = -(-terms * terms // voxels)
    gram_flat = jnp.pad(gram_matrix.reshape(terms * terms), (0, gram_rows * voxels - terms * terms))
    packed = jnp.concatenate([cross_products, gram_flat.reshape(gram_rows, voxels)], axis=0)
    summed = sum_over_tm(packed)
    cross_products = summed[:terms]
    gram_matrix = summed[terms:].reshape(-1)[: terms * terms].reshape(terms, terms)
    factor = jnp.linalg.cholesky(gram_matrix)
    weights = jax.scipy.linalg.cho_solve((factor, True), nuisance_matrix.T)
    return spike_free_series - precise_product(weights.T, cross_products)


def solution(mesh):
    return jax.shard_map(
        local,
        mesh=mesh,
        in_specs=(P("tm", "vox"), P("tm", "vox"), P("tm", None), P(None, "vox")),
        out_specs=P("tm", "vox"),
        check_vma=False,
    )
```

```python
import jax
import jax.numpy as jnp
from jax import lax
from jax.sharding import PartitionSpec as P

LEVELS = 4
HALO = 16


def from_behind(block, axis, distance):
    devices = range(lax.axis_size(axis))
    route = [((i - distance) % len(devices), i) for i in devices]
    return lax.ppermute(block, axis, route)


def precise_product(left, right):
    return jnp.dot(left, right, precision=lax.Precision.HIGHEST, preferred_element_type=jnp.float32)


def keep_level(spikes, level):
    return 1.0 - (spikes // 2**level % 2).astype(jnp.float32)


def despike_trimmed(window, flags):
    length = window.shape[0]
    approx = window
    start = 0
    kept_list = []
    for level in range(LEVELS):
        shift_rows = 2**level
        current, lagged = approx[shift_rows:], approx[:-shift_rows]
        start += shift_rows
        keep = keep_level(flags[start:], level)
        kept_list.append((start, (current - lagged) * 0.5 * keep))
        approx = (current + lagged) * 0.5
    for level in range(LEVELS - 1, -1, -1):
        shift_rows = 2**level
        kept_start, kept = kept_list[level]
        kept = kept[start - kept_start : start - kept_start + approx.shape[0]]
        approx = (approx[:-shift_rows] + approx[shift_rows:]) * 0.5 + (kept[:-shift_rows] - kept[shift_rows:]) * 0.5
    return approx


def sum_over_vox(block):
    n = lax.axis_size("vox")
    flat = block.reshape(1, block.size)
    copies = jnp.broadcast_to(flat, (n,) + flat.shape)
    return lax.all_to_all(copies, "vox", 0, 0, tiled=False).sum(axis=0).reshape(block.shape)


def sum_over_tm(block):
    n = lax.axis_size("tm")
    rows, cols = block.shape
    parts = block.reshape(rows, n, cols // n).transpose(1, 0, 2)
    owned = lax.all_to_all(parts, "tm", 0, 0, tiled=False).sum(axis=0)
    copies = jnp.broadcast_to(owned, (n,) + owned.shape)
    gathered = lax.all_to_all(copies, "tm", 0, 0, tiled=False)
    return gathered.transpose(1, 0, 2).reshape(rows, cols)


def local(series, spikes, motion, tissue):
    frames = series.shape[0]
    voxels = series.shape[1]
    motion_row = jnp.pad(motion[frames - 1 :], ((0, 7), (0, voxels - motion.shape[1])))
    tail = jnp.concatenate([series[frames - HALO :], spikes[frames - HALO :].astype(jnp.float32), motion_row], axis=0)
    head = jnp.concatenate([series[:HALO], spikes[:HALO].astype(jnp.float32)], axis=0)
    before = from_behind(tail, "tm", 1)
    after = from_behind(head, "tm", -1)
    motion_before = before[2 * HALO : 2 * HALO + 1, : motion.shape[1]]
    inner = despike_trimmed(series, spikes)
    edge = 2 * HALO
    head_window = despike_trimmed(
        jnp.concatenate([before[:HALO], series[:edge]], axis=0),
        jnp.concatenate([before[HALO : 2 * HALO].astype(jnp.int32), spikes[:edge]], axis=0),
    )
    tail_window = despike_trimmed(
        jnp.concatenate([series[frames - edge :], after[:HALO]], axis=0),
        jnp.concatenate([spikes[frames - edge :], after[HALO:].astype(jnp.int32)], axis=0),
    )
    spike_free_series = jnp.concatenate([head_window[1 : HALO + 1], inner[1 : frames - 31], tail_window[1 : HALO + 1]], axis=0)

    rows = jnp.concatenate([head_window[:1], spike_free_series], axis=0)
    numer = sum_over_vox(precise_product(rows, tissue.T))
    voxel_signals = jnp.pad(numer, ((7, 0), (0, 0))) / float(tissue.shape[1] * lax.axis_size("vox"))

    first = lax.axis_index("tm") == 0
    base_before = jnp.concatenate([motion_before, voxel_signals[7:8]], axis=1)
    base_before = jnp.where(first, jnp.zeros_like(base_before), base_before)
    base_regressors = jnp.concatenate([motion, voxel_signals[8:]], axis=1)
    previous = jnp.concatenate([base_before, base_regressors[:-1]], axis=0)
    temporal_derivative = base_regressors - previous
    nuisance_matrix = jnp.concatenate(
        [
            base_regressors,
            temporal_derivative,
            base_regressors * base_regressors,
            temporal_derivative * temporal_derivative,
        ],
        axis=1,
    )
    terms = nuisance_matrix.shape[1]
    gram_matrix = precise_product(nuisance_matrix.T, nuisance_matrix)
    cross_products = precise_product(nuisance_matrix.T, spike_free_series)
    gram_rows = -(-terms * terms // voxels)
    gram_flat = jnp.pad(gram_matrix.reshape(terms * terms), (0, gram_rows * voxels - terms * terms))
    packed = jnp.concatenate([cross_products, gram_flat.reshape(gram_rows, voxels)], axis=0)
    summed = sum_over_tm(packed)
    cross_products = summed[:terms]
    gram_matrix = summed[terms:].reshape(-1)[: terms * terms].reshape(terms, terms)
    factor = lax.linalg.cholesky(gram_matrix, symmetrize_input=False)
    weights = jax.scipy.linalg.cho_solve((factor, True), nuisance_matrix.T)
    return spike_free_series - precise_product(weights.T, cross_products)


def solution(mesh):
    return jax.shard_map(
        local,
        mesh=mesh,
        in_specs=(P("tm", "vox"), P("tm", "vox"), P("tm", None), P(None, "vox")),
        out_specs=P("tm", "vox"),
        check_vma=False,
    )
```
